128 devices in a mesh: dp: 32 (over z, x, core), tensor: 4 (over y).
Axes of the slice: x: 4, y: 4, z: 4, core: 2. Of those that a mesh axis runs over, the one named last changes fastest.
Arguments:
- normed_hidden_state: bfloat16 [4, 2048, 8192], P(None, 'dp', 'tensor'), may hold values from -6 to 6
- query_projection_weight: bfloat16 [8192, 4096], P(None, 'tensor'), may hold values from -0.0625 to 0.0625
- adapter_down_maps: bfloat16 [4096, 8192], P('dp', 'tensor'), may hold values from -0.0625 to 0.0625
- adapter_up_maps: bfloat16 [4096, 4096], P('dp', 'tensor'), may hold values from -0.75 to 0.75
- key_value_cache: bfloat16 [2, 2048, 128, 512], P(None, 'dp', None, 'tensor'), may hold values from -82 to 82
- step_key_value: bfloat16 [4, 2, 2048, 512], P(None, None, 'dp', 'tensor'), may hold values from -6 to 6
- cache_valid_length: int32 [2048], P('dp'), may hold values from 1 to 128, as said below
- adapter_per_request: int32 [2048], P('dp'), may hold values from 0 to 63, as said below
- adapter_pool_position: int32 [64], replicated, may hold values from 0 to 63, as said below
Outputs:
- attended: bfloat16 [4, 2048, 4096], P(None, 'dp', 'tensor')
The draws below stay inside these ranges and needn't reach their ends.
Inputs may be any that keep to these rules, and one draw needn't show every extreme that they name: `adapter_pool_position`: A permutation: every adapter has its own pool position, and position p is held by dp index p // 2. `adapter_per_request`: within each group of 64 consecutive requests, requests whose adapters sit on the same dp index use the same adapter; some dp index serves an adapter to every group. `cache_valid_length`: each group of 64 consecutive requests holds a request with all 128 positions valid.
All inputs are finite; a program needn't handle non-finite values.
Results may differ from the reference program's by a relative error of at most 0.015.
Values may be sent and summed in bfloat16 or wider, within the bound.
No kernel may reach another device: no remote copies, remote signals or barrier semaphores. Data moves between devices by JAX's collectives and lax.ppermute only.
A program may use at most 192 MiB of HBM per device.

```python
import math
import jax
import jax.numpy as jnp
from jax import lax

MODEL_WIDTH = 8192
HEADS = 32
KV_HEADS = 4
HEAD_SIZE = 128
ADAPTER_RANK = 64
STEPS = 4
POOL_DEV = 2
REQ_GRP = 64
CACHE = 128
QUERY_FEATURES = 4096
KVW = 512
REQS = 2048
ADAPTER_POOL = 64


def pool_order(key):
    return jax.random.permutation(jax.random.fold_in(key, 11), ADAPTER_POOL).astype(jnp.int32)


def draw_adapter_pool_position(key, part):
    return pool_order(key)


def draw_adapter_per_request(key, part):
    groups = REQS // REQ_GRP
    order = pool_order(key)
    inverse = jnp.argsort(order).astype(jnp.int32)
    owner = jax.random.randint(jax.random.fold_in(key, 12), (groups, REQ_GRP), 0, groups).astype(jnp.int32)
    common = jax.random.randint(jax.random.fold_in(key, 13), (), 0, groups).astype(jnp.int32)
    chosen = jax.random.randint(jax.random.fold_in(key, 14), (groups,), 0, REQ_GRP).astype(jnp.int32)
    owner = jnp.where(jnp.arange(REQ_GRP, dtype=jnp.int32)[None, :] == chosen[:, None], common, owner)
    slot_table = jax.random.randint(jax.random.fold_in(key, 15), (groups, groups), 0, POOL_DEV).astype(jnp.int32)
    picked = jnp.take_along_axis(slot_table, owner, axis=1)
    spot = owner * POOL_DEV + picked
    return jnp.take(inverse, spot.reshape(-1), axis=0).astype(jnp.int32)


def draw_cache_valid_length(key, part):
    groups = REQS // REQ_GRP
    lengths = jax.random.randint(jax.random.fold_in(key, 21), (groups, REQ_GRP), 1, CACHE + 1).astype(jnp.int32)
    chosen = jax.random.randint(jax.random.fold_in(key, 22), (groups,), 0, REQ_GRP).astype(jnp.int32)
    lengths = jnp.where(jnp.arange(REQ_GRP, dtype=jnp.int32)[None, :] == chosen[:, None], CACHE, lengths)
    return lengths.reshape(-1).astype(jnp.int32)


def draw_key_value_cache(key, part):
    shape = (2, REQS, CACHE, KVW)
    result = jnp.clip(jax.random.normal(jax.random.fold_in(key, 34), shape, jnp.float32), -4.0, 4.0)
    return result.astype(jnp.bfloat16)


def block_levels(own_key, dims, pieces, low, top_value):
    factor_of = 1.0
    for dim, shards_of in pieces:
        steps = jax.random.uniform(jax.random.fold_in(jax.random.fold_in(own_key, 6), dim), (shards_of,), jnp.float32, low / len(pieces), top_value / len(pieces))
        factor_of = factor_of * jnp.repeat(jnp.exp(steps), dims[dim] // shards_of).reshape((-1,) + (1,) * (len(dims) - 1 - dim))
    return factor_of


def scatter_about(rng, shape, scale, limit, pieces=(), kind=jnp.bfloat16):
    entries = jax.random.normal(rng, shape, jnp.float32) * scale
    if len(pieces) > 0:
        entries = block_levels(rng, shape, pieces, -0.22, 0.18) * entries
    return jnp.clip(entries, min=-limit, max=limit).astype(kind)


def setup_inputs(seed: int = 0) -> dict:
    key_of = jax.random.split(jax.random.key(seed), 10)
    return {
        "normed_hidden_state": scatter_about(key_of[0], (STEPS, REQS, MODEL_WIDTH), 1.0, 6.0, ((1, 32), (2, 4))),
        "query_projection_weight": scatter_about(key_of[1], (MODEL_WIDTH, QUERY_FEATURES), MODEL_WIDTH ** -0.5, 0.0625, ((1, 4),)),
        "adapter_down_maps": scatter_about(key_of[2], (ADAPTER_POOL * ADAPTER_RANK, MODEL_WIDTH), MODEL_WIDTH ** -0.5, 0.0625, ((0, 32), (1, 4))),
        "adapter_up_maps": scatter_about(key_of[3], (ADAPTER_POOL * ADAPTER_RANK, QUERY_FEATURES), ADAPTER_RANK ** -0.5, 0.75, ((0, 32), (1, 4))),
        "key_value_cache": draw_key_value_cache(jax.random.fold_in(key_of[9], 71), 0),
        "step_key_value": scatter_about(key_of[5], (STEPS, 2, REQS, KVW), 1.0, 6.0, ((2, 32), (3, 4))),
        "cache_valid_length": draw_cache_valid_length(jax.random.fold_in(key_of[9], 71), 0),
        "adapter_per_request": draw_adapter_per_request(jax.random.fold_in(key_of[9], 71), 0),
        "adapter_pool_position": draw_adapter_pool_position(jax.random.fold_in(key_of[9], 71), 0),
    }


def reference(normed_hidden_state, query_projection_weight, adapter_down_maps, adapter_up_maps, key_value_cache, step_key_value, cache_valid_length, adapter_per_request, adapter_pool_position):
    position = jnp.take(adapter_pool_position, adapter_per_request, axis=0).astype(jnp.int32)
    token_rows = normed_hidden_state.reshape(STEPS * REQS, MODEL_WIDTH)
    base = jnp.dot(token_rows, query_projection_weight, preferred_element_type=jnp.float32).reshape(STEPS, REQS, QUERY_FEATURES)
    down_map_pages = adapter_down_maps.reshape(ADAPTER_POOL, ADAPTER_RANK, MODEL_WIDTH)
    up_map_pages = adapter_up_maps.reshape(ADAPTER_POOL, ADAPTER_RANK, QUERY_FEATURES)

    def adapt_one(item):
        request_rows, spot = item
        down_page = down_map_pages[spot]
        up_page = up_map_pages[spot]
        shrink = lax.dot_general(request_rows, down_page, (((1,), (1,)), ((), ())), preferred_element_type=jnp.float32)
        shrink = shrink.astype(jnp.bfloat16)
        return jnp.dot(shrink, up_page, preferred_element_type=jnp.float32)
    delta = lax.map(adapt_one, (jnp.transpose(normed_hidden_state, (1, 0, 2)), position))
    query = (base + jnp.transpose(delta, (1, 0, 2))).astype(jnp.bfloat16)
    group = HEADS // KV_HEADS
    scale = 1.0 / math.sqrt(HEAD_SIZE)
    grouped = query.astype(jnp.float32).reshape(STEPS, REQS, KV_HEADS, group, HEAD_SIZE)
    keys = key_value_cache[0].astype(jnp.float32).reshape(REQS, CACHE, KV_HEADS, HEAD_SIZE)
    values = key_value_cache[1].astype(jnp.float32).reshape(REQS, CACHE, KV_HEADS, HEAD_SIZE)
    new_keys = step_key_value[:, 0].astype(jnp.float32).reshape(STEPS, REQS, KV_HEADS, HEAD_SIZE)
    new_values = step_key_value[:, 1].astype(jnp.float32).reshape(STEPS, REQS, KV_HEADS, HEAD_SIZE)
    cache_scores = jnp.einsum('trkgd,rckd->trkgc', grouped, keys) * scale
    valid = jnp.arange(CACHE, dtype=jnp.int32)[None, :] < cache_valid_length[:, None]
    cache_scores = jnp.where(valid[None, :, None, None, :], cache_scores, -1e+30)
    fresh_scores = jnp.einsum('trkgd,srkd->trkgs', grouped, new_keys) * scale
    causal = jnp.arange(STEPS, dtype=jnp.int32)[:, None] >= jnp.arange(STEPS, dtype=jnp.int32)[None, :]
    fresh_scores = jnp.where(causal[:, None, None, None, :], fresh_scores, -1e+30)
    top = jnp.maximum(lax.optimization_barrier(jnp.max(cache_scores, axis=-1)), lax.optimization_barrier(jnp.max(fresh_scores, axis=-1)))
    cache_expo = jnp.exp(cache_scores - top[..., None])
    fresh_expo = jnp.exp(fresh_scores - top[..., None])
    total = lax.optimization_barrier(jnp.sum(cache_expo, axis=-1)) + lax.optimization_barrier(jnp.sum(fresh_expo, axis=-1))
    cache_weights = lax.optimization_barrier(cache_expo.astype(jnp.bfloat16)).astype(jnp.float32)
    fresh_weights = lax.optimization_barrier(fresh_expo.astype(jnp.bfloat16)).astype(jnp.float32)
    mixed = jnp.einsum('trkgc,rckd->trkgd', cache_weights, values)
    mixed = mixed + jnp.einsum('trkgs,srkd->trkgd', fresh_weights, new_values)
    attended = mixed / total[..., None]
    return attended.reshape(STEPS, REQS, QUERY_FEATURES).astype(jnp.bfloat16)
```

```python
import math

import jax
import jax.numpy as jnp
import numpy as np
from jax import lax
from jax.sharding import Mesh
from jax.sharding import PartitionSpec as P

HEAD_SIZE = 128
ADAPTER_RANK = 64
CORES = 2


def pool_lookup(adapters, adapter_pool_position):
    table = jnp.arange(adapter_pool_position.shape[0], dtype=jnp.int32)
    match = adapters[:, None] == table[None, :]
    return jnp.sum(jnp.where(match, adapter_pool_position[None, :], 0), axis=1)


def shift_all(value, axis, count):
    pieces = [value]
    for k in range(1, count):
        pieces.append(lax.ppermute(value, axis, [(i, (i + k) % count) for i in range(count)]))
    return pieces


def attend(query, key_value_cache, step_key_value, cache_valid_length):
    steps = step_key_value.shape[0]
    requests = step_key_value.shape[2]
    length = key_value_cache.shape[2]
    kv_local = key_value_cache.shape[3] // HEAD_SIZE
    group = query.shape[2] // HEAD_SIZE // kv_local
    scale = 1.0 / math.sqrt(HEAD_SIZE)
    grouped = query.reshape(steps, requests, kv_local, group, HEAD_SIZE)
    keys = key_value_cache[0].reshape(requests, length, kv_local, HEAD_SIZE)
    values = key_value_cache[1].reshape(requests, length, kv_local, HEAD_SIZE)
    new_keys = step_key_value[:, 0].reshape(steps, requests, kv_local, HEAD_SIZE)
    new_values = step_key_value[:, 1].reshape(steps, requests, kv_local, HEAD_SIZE)
    cache_scores = (
        jnp.einsum("trkgd,rckd->trkgc", grouped, keys, preferred_element_type=jnp.float32) * scale
    )
    valid = jnp.arange(length, dtype=jnp.int32)[None, :] < cache_valid_length[:, None]
    cache_scores = jnp.where(valid[None, :, None, None, :], cache_scores, -1e30)
    fresh_scores = (
        jnp.einsum("trkgd,srkd->trkgs", grouped, new_keys, preferred_element_type=jnp.float32)
        * scale
    )
    causal = (
        jnp.arange(steps, dtype=jnp.int32)[:, None] >= jnp.arange(steps, dtype=jnp.int32)[None, :]
    )
    fresh_scores = jnp.where(causal[:, None, None, None, :], fresh_scores, -1e30)
    top = jnp.maximum(jnp.max(cache_scores, axis=-1), jnp.max(fresh_scores, axis=-1))
    cache_expo = jnp.exp(cache_scores - top[..., None])
    fresh_expo = jnp.exp(fresh_scores - top[..., None])
    total = jnp.sum(cache_expo, axis=-1) + jnp.sum(fresh_expo, axis=-1)
    mixed = jnp.einsum(
        "trkgc,rckd->trkgd",
        cache_expo.astype(jnp.bfloat16),
        values,
        preferred_element_type=jnp.float32,
    )
    mixed = mixed + jnp.einsum(
        "trkgs,srkd->trkgd",
        fresh_expo.astype(jnp.bfloat16),
        new_values,
        preferred_element_type=jnp.float32,
    )
    attended = mixed / total[..., None]
    return attended.reshape(steps, requests, -1).astype(jnp.bfloat16)


def per_device(
    normed_hidden_state,
    query_projection_weight,
    adapter_down_maps,
    adapter_up_maps,
    key_value_cache,
    step_key_value,
    cache_valid_length,
    adapter_per_request,
    adapter_pool_position,
):
    steps, requests, part_width = normed_hidden_state.shape
    count_rows = steps * requests
    heads_width = query_projection_weight.shape[1]
    n_tensor = query_projection_weight.shape[0] // part_width
    pool_dev = adapter_down_maps.shape[0] // ADAPTER_RANK
    token_rows = normed_hidden_state.reshape(count_rows, part_width)

    down_mine = lax.all_gather(adapter_down_maps, "chip", axis=0, tiled=True)
    up_mine = lax.all_gather(adapter_up_maps, "chip", axis=0, tiled=True)
    swap = [(0, 1), (1, 0)]
    down_other = lax.ppermute(down_mine, "core", swap)
    up_other = lax.ppermute(up_mine, "core", swap)
    n_slots = down_mine.shape[0] // ADAPTER_RANK

    t = lax.axis_index("tensor")
    pieces = shift_all(token_rows, "tensor", n_tensor)
    base = None
    for k, piece in enumerate(pieces):
        src = (t - k) % n_tensor
        w_rows = lax.dynamic_slice_in_dim(query_projection_weight, src * part_width, part_width, 0)
        part = jnp.dot(piece, w_rows, preferred_element_type=jnp.float32)
        base = part if base is None else base + part

    position = pool_lookup(adapter_per_request, adapter_pool_position)
    my_core = lax.axis_index("core")
    holder = position // pool_dev
    slot_index = (holder // CORES) * pool_dev + position % pool_dev
    on_mine = (holder % CORES) == my_core
    slots = jnp.arange(n_slots, dtype=jnp.int32)[None, :]
    mask_mine = on_mine[:, None] & (slot_index[:, None] == slots)
    mask_other = (~on_mine)[:, None] & (slot_index[:, None] == slots)

    def shrink_part(down_block, mask):
        full = lax.dot_general(
            token_rows, down_block, (((1,), (1,)), ((), ())), preferred_element_type=jnp.float32
        ).reshape(steps, requests, n_slots, ADAPTER_RANK)
        return jnp.sum(jnp.where(mask[None, :, :, None], full, 0.0), axis=2)

    shrink_local = shrink_part(down_mine, mask_mine) + shrink_part(down_other, mask_other)
    partials = shift_all(shrink_local, "tensor", n_tensor)
    shrink_sum = partials[0]
    for p in partials[1:]:
        shrink_sum = shrink_sum + p
    shrink = shrink_sum.astype(jnp.bfloat16)

    def expand(mask):
        wide = jnp.where(mask[None, :, :, None], shrink[:, :, None, :], jnp.zeros((), jnp.bfloat16))
        return wide.reshape(count_rows, n_slots * ADAPTER_RANK)

    delta = jnp.dot(expand(mask_mine), up_mine, preferred_element_type=jnp.float32) + jnp.dot(
        expand(mask_other), up_other, preferred_element_type=jnp.float32
    )
    query = (base + delta).reshape(steps, requests, heads_width).astype(jnp.bfloat16)
    return attend(query, key_value_cache, step_key_value, cache_valid_length)


def solution(mesh):
    devices = np.asarray(mesh.devices)
    n_dp, n_tensor = devices.shape
    grid = Mesh(devices.reshape(n_dp // CORES, CORES, n_tensor), ("chip", "core", "tensor"))
    dp = ("chip", "core")
    return jax.shard_map(
        per_device,
        mesh=grid,
        in_specs=(
            P(None, dp, "tensor"),
            P(None, "tensor"),
            P(dp, "tensor"),
            P(dp, "tensor"),
            P(None, dp, None, "tensor"),
            P(None, None, dp, "tensor"),
            P(dp),
            P(dp),
            P(),
        ),
        out_specs=P(None, dp, "tensor"),
        check_vma=False,
    )
```

```python
import math

import jax
import jax.numpy as jnp
from jax import lax
from jax.sharding import PartitionSpec as P

HEAD_SIZE = 128
ADAPTER_RANK = 64


def pool_lookup(adapters, adapter_pool_position):
    table = jnp.arange(adapter_pool_position.shape[0], dtype=jnp.int32)
    match = adapters[:, None] == table[None, :]
    return jnp.sum(jnp.where(match, adapter_pool_position[None, :], 0), axis=1)


def attend(query, key_value_cache, step_key_value, cache_valid_length):
    steps = step_key_value.shape[0]
    requests = step_key_value.shape[2]
    length = key_value_cache.shape[2]
    kv_local = key_value_cache.shape[3] // HEAD_SIZE
    group = query.shape[2] // HEAD_SIZE // kv_local
    scale = 1.0 / math.sqrt(HEAD_SIZE)
    grouped = query.reshape(steps, requests, kv_local, group, HEAD_SIZE)
    keys = key_value_cache[0].reshape(requests, length, kv_local, HEAD_SIZE)
    values = key_value_cache[1].reshape(requests, length, kv_local, HEAD_SIZE)
    new_keys = step_key_value[:, 0].reshape(steps, requests, kv_local, HEAD_SIZE)
    new_values = step_key_value[:, 1].reshape(steps, requests, kv_local, HEAD_SIZE)
    cache_scores = (
        jnp.einsum("trkgd,rckd->trkgc", grouped, keys, preferred_element_type=jnp.float32) * scale
    )
    valid = jnp.arange(length, dtype=jnp.int32)[None, :] < cache_valid_length[:, None]
    cache_scores = jnp.where(valid[None, :, None, None, :], cache_scores, -1e30)
    fresh_scores = (
        jnp.einsum("trkgd,srkd->trkgs", grouped, new_keys, preferred_element_type=jnp.float32)
        * scale
    )
    causal = (
        jnp.arange(steps, dtype=jnp.int32)[:, None] >= jnp.arange(steps, dtype=jnp.int32)[None, :]
    )
    fresh_scores = jnp.where(causal[:, None, None, None, :], fresh_scores, -1e30)
    top = jnp.maximum(jnp.max(cache_scores, axis=-1), jnp.max(fresh_scores, axis=-1))
    cache_expo = jnp.exp(cache_scores - top[..., None])
    fresh_expo = jnp.exp(fresh_scores - top[..., None])
    total = jnp.sum(cache_expo, axis=-1) + jnp.sum(fresh_expo, axis=-1)
    mixed = jnp.einsum(
        "trkgc,rckd->trkgd",
        cache_expo.astype(jnp.bfloat16),
        values,
        preferred_element_type=jnp.float32,
    )
    mixed = mixed + jnp.einsum(
        "trkgs,srkd->trkgd",
        fresh_expo.astype(jnp.bfloat16),
        new_values,
        preferred_element_type=jnp.float32,
    )
    attended = mixed / total[..., None]
    return attended.reshape(steps, requests, -1).astype(jnp.bfloat16)


def gather_tensor(value, axis_name, count):
    tiled = jnp.broadcast_to(value[None], (count,) + value.shape)
    return lax.all_to_all(tiled, axis_name, 0, 0, tiled=True)


def per_device(
    normed_hidden_state,
    query_projection_weight,
    adapter_down_maps,
    adapter_up_maps,
    key_value_cache,
    step_key_value,
    cache_valid_length,
    adapter_per_request,
    adapter_pool_position,
):
    steps, requests, part_width = normed_hidden_state.shape
    count_rows = steps * requests
    heads_width = query_projection_weight.shape[1]
    n_tensor = query_projection_weight.shape[0] // part_width
    token_rows = normed_hidden_state.reshape(count_rows, part_width)

    down_all = lax.all_gather(adapter_down_maps, "dp", axis=0, tiled=True)
    up_all = lax.all_gather(adapter_up_maps, "dp", axis=0, tiled=True)
    n_pool = down_all.shape[0] // ADAPTER_RANK

    pieces = gather_tensor(token_rows, "tensor", n_tensor)
    full_rows = jnp.transpose(pieces, (1, 0, 2)).reshape(count_rows, n_tensor * part_width)
    base = jnp.dot(full_rows, query_projection_weight, preferred_element_type=jnp.float32)

    position = pool_lookup(adapter_per_request, adapter_pool_position)
    onehot = position[:, None] == jnp.arange(n_pool, dtype=jnp.int32)[None, :]
    full = lax.dot_general(
        token_rows, down_all, (((1,), (1,)), ((), ())), preferred_element_type=jnp.float32
    ).reshape(steps, requests, n_pool, ADAPTER_RANK)
    shrink_local = jnp.sum(jnp.where(onehot[None, :, :, None], full, 0.0), axis=2)
    partials = gather_tensor(shrink_local, "tensor", n_tensor)
    shrink = partials[0]
    for j in range(1, n_tensor):
        shrink = shrink + partials[j]
    shrink = shrink.astype(jnp.bfloat16)
    wide = jnp.where(onehot[None, :, :, None], shrink[:, :, None, :], jnp.zeros((), jnp.bfloat16))
    delta = jnp.dot(
        wide.reshape(count_rows, n_pool * ADAPTER_RANK), up_all, preferred_element_type=jnp.float32
    )
    query = (base + delta).reshape(steps, requests, heads_width).astype(jnp.bfloat16)
    return attend(query, key_value_cache, step_key_value, cache_valid_length)


def solution(mesh):
    return jax.shard_map(
        per_device,
        mesh=mesh,
        in_specs=(
            P(None, "dp", "tensor"),
            P(None, "tensor"),
            P("dp", "tensor"),
            P("dp", "tensor"),
            P(None, "dp", None, "tensor"),
            P(None, None, "dp", "tensor"),
            P("dp"),
            P("dp"),
            P(),
        ),
        out_specs=P(None, "dp", "tensor"),
        check_vma=False,
    )
```

```python
import math

import jax
import jax.numpy as jnp
from jax import lax
from jax.sharding import PartitionSpec as P

HEAD_SIZE = 128
ADAPTER_RANK = 64


def pool_lookup(adapters, adapter_pool_position):
    table = jnp.arange(adapter_pool_position.shape[0], dtype=jnp.int32)
    match = adapters[:, None] == table[None, :]
    return jnp.sum(jnp.where(match, adapter_pool_position[None, :], 0), axis=1)


def attend(query, key_value_cache, step_key_value, cache_valid_length):
    steps = step_key_value.shape[0]
    requests = step_key_value.shape[2]
    length = key_value_cache.shape[2]
    kv_local = key_value_cache.shape[3] // HEAD_SIZE
    group = query.shape[2] // HEAD_SIZE // kv_local
    scale = 1.0 / math.sqrt(HEAD_SIZE)
    grouped = query.reshape(steps, requests, kv_local, group, HEAD_SIZE)
    keys = key_value_cache[0].reshape(requests, length, kv_local, HEAD_SIZE)
    values = key_value_cache[1].reshape(requests, length, kv_local, HEAD_SIZE)
    new_keys = step_key_value[:, 0].reshape(steps, requests, kv_local, HEAD_SIZE)
    new_values = step_key_value[:, 1].reshape(steps, requests, kv_local, HEAD_SIZE)
    cache_scores = (
        jnp.einsum("trkgd,rckd->trkgc", grouped, keys, preferred_element_type=jnp.float32) * scale
    )
    valid = jnp.arange(length, dtype=jnp.int32)[None, :] < cache_valid_length[:, None]
    cache_scores = jnp.where(valid[None, :, None, None, :], cache_scores, -1e30)
    fresh_scores = (
        jnp.einsum("trkgd,srkd->trkgs", grouped, new_keys, preferred_element_type=jnp.float32)
        * scale
    )
    causal = (
        jnp.arange(steps, dtype=jnp.int32)[:, None] >= jnp.arange(steps, dtype=jnp.int32)[None, :]
    )
    fresh_scores = jnp.where(causal[:, None, None, None, :], fresh_scores, -1e30)
    top = jnp.maximum(jnp.max(cache_scores, axis=-1), jnp.max(fresh_scores, axis=-1))
    cache_expo = jnp.exp(cache_scores - top[..., None])
    fresh_expo = jnp.exp(fresh_scores - top[..., None])
    total = jnp.sum(cache_expo, axis=-1) + jnp.sum(fresh_expo, axis=-1)
    mixed = jnp.einsum(
        "trkgc,rckd->trkgd",
        cache_expo.astype(jnp.bfloat16),
        values,
        preferred_element_type=jnp.float32,
    )
    mixed = mixed + jnp.einsum(
        "trkgs,srkd->trkgd",
        fresh_expo.astype(jnp.bfloat16),
        new_values,
        preferred_element_type=jnp.float32,
    )
    attended = mixed / total[..., None]
    return attended.reshape(steps, requests, -1).astype(jnp.bfloat16)


def gather_tensor(value, axis_name, count):
    tiled = jnp.broadcast_to(value[None], (count,) + value.shape)
    return lax.all_to_all(tiled, axis_name, 0, 0, tiled=True)


def per_device(
    normed_hidden_state,
    query_projection_weight,
    adapter_down_maps,
    adapter_up_maps,
    key_value_cache,
    step_key_value,
    cache_valid_length,
    adapter_per_request,
    adapter_pool_position,
):
    steps, requests, part_width = normed_hidden_state.shape
    count_rows = steps * requests
    heads_width = query_projection_weight.shape[1]
    n_tensor = query_projection_weight.shape[0] // part_width
    token_rows = normed_hidden_state.reshape(count_rows, part_width)

    down_all = lax.all_gather(adapter_down_maps, "dp", axis=0, tiled=True)
    n_pool = down_all.shape[0] // ADAPTER_RANK

    pieces = gather_tensor(token_rows, "tensor", n_tensor)
    full_rows = jnp.transpose(pieces, (1, 0, 2)).reshape(count_rows, n_tensor * part_width)
    base = jnp.dot(full_rows, query_projection_weight, preferred_element_type=jnp.float32)

    up_local, down_all, base = lax.optimization_barrier((adapter_up_maps, down_all, base))
    up_all = lax.all_gather(up_local, "dp", axis=0, tiled=True)

    position = pool_lookup(adapter_per_request, adapter_pool_position)
    onehot = position[:, None] == jnp.arange(n_pool, dtype=jnp.int32)[None, :]
    full = lax.dot_general(
        token_rows, down_all, (((1,), (1,)), ((), ())), preferred_element_type=jnp.float32
    ).reshape(steps, requests, n_pool, ADAPTER_RANK)
    shrink_local = jnp.sum(jnp.where(onehot[None, :, :, None], full, 0.0), axis=2)
    partials = gather_tensor(shrink_local, "tensor", n_tensor)
    shrink = partials[0]
    for j in range(1, n_tensor):
        shrink = shrink + partials[j]
    shrink = shrink.astype(jnp.bfloat16)
    wide = jnp.where(onehot[None, :, :, None], shrink[:, :, None, :], jnp.zeros((), jnp.bfloat16))
    delta = jnp.dot(
        wide.reshape(count_rows, n_pool * ADAPTER_RANK), up_all, preferred_element_type=jnp.float32
    )
    query = (base + delta).reshape(steps, requests, heads_width).astype(jnp.bfloat16)
    return attend(query, key_value_cache, step_key_value, cache_valid_length)


def solution(mesh):
    return jax.shard_map(
        per_device,
        mesh=mesh,
        in_specs=(
            P(None, "dp", "tensor"),
            P(None, "tensor"),
            P("dp", "tensor"),
            P("dp", "tensor"),
            P(None, "dp", None, "tensor"),
            P(None, None, "dp", "tensor"),
            P("dp"),
            P("dp"),
            P(),
        ),
        out_specs=P(None, "dp", "tensor"),
        check_vma=False,
    )
```

```python
import math

import jax
import jax.numpy as jnp
from jax import lax
from jax.sharding import PartitionSpec as P

HEAD_SIZE = 128
ADAPTER_RANK = 64


def pool_lookup(adapters, adapter_pool_position):
    table = jnp.arange(adapter_pool_position.shape[0], dtype=jnp.int32)
    match = adapters[:, None] == table[None, :]
    return jnp.sum(jnp.where(match, adapter_pool_position[None, :], 0), axis=1)


def attend(query, key_value_cache, step_key_value, cache_valid_length):
    steps = step_key_value.shape[0]
    requests = step_key_value.shape[2]
    length = key_value_cache.shape[2]
    kv_local = key_value_cache.shape[3] // HEAD_SIZE
    group = query.shape[2] // HEAD_SIZE // kv_local
    scale = 1.0 / math.sqrt(HEAD_SIZE)
    grouped = query.reshape(steps, requests, kv_local, group, HEAD_SIZE)
    keys = key_value_cache[0].reshape(requests, length, kv_local, HEAD_SIZE)
    values = key_value_cache[1].reshape(requests, length, kv_local, HEAD_SIZE)
    new_keys = step_key_value[:, 0].reshape(steps, requests, kv_local, HEAD_SIZE)
    new_values = step_key_value[:, 1].reshape(steps, requests, kv_local, HEAD_SIZE)
    cache_scores = (
        jnp.einsum("trkgd,rckd->trkgc", grouped, keys, preferred_element_type=jnp.float32) * scale
    )
    valid = jnp.arange(length, dtype=jnp.int32)[None, :] < cache_valid_length[:, None]
    cache_scores = jnp.where(valid[None, :, None, None, :], cache_scores, -1e30)
    fresh_scores = (
        jnp.einsum("trkgd,srkd->trkgs", grouped, new_keys, preferred_element_type=jnp.float32)
        * scale
    )
    causal = (
        jnp.arange(steps, dtype=jnp.int32)[:, None] >= jnp.arange(steps, dtype=jnp.int32)[None, :]
    )
    fresh_scores = jnp.where(causal[:, None, None, None, :], fresh_scores, -1e30)
    top = jnp.maximum(jnp.max(cache_scores, axis=-1), jnp.max(fresh_scores, axis=-1))
    cache_expo = jnp.exp(cache_scores - top[..., None])
    fresh_expo = jnp.exp(fresh_scores - top[..., None])
    total = jnp.sum(cache_expo, axis=-1) + jnp.sum(fresh_expo, axis=-1)
    mixed = jnp.einsum(
        "trkgc,rckd->trkgd",
        cache_expo.astype(jnp.bfloat16),
        values,
        preferred_element_type=jnp.float32,
    )
    mixed = mixed + jnp.einsum(
        "trkgs,srkd->trkgd",
        fresh_expo.astype(jnp.bfloat16),
        new_values,
        preferred_element_type=jnp.float32,
    )
    attended = mixed / total[..., None]
    return attended.reshape(steps, requests, -1).astype(jnp.bfloat16)


def gather_tensor(value, axis_name, count):
    tiled = jnp.broadcast_to(value[None], (count,) + value.shape)
    return lax.all_to_all(tiled, axis_name, 0, 0, tiled=True)


def per_device(
    normed_hidden_state,
    query_projection_weight,
    adapter_down_maps,
    adapter_up_maps,
    key_value_cache,
    step_key_value,
    cache_valid_length,
    adapter_per_request,
    adapter_pool_position,
):
    steps, requests, part_width = normed_hidden_state.shape
    count_rows = steps * requests
    heads_width = query_projection_weight.shape[1]
    n_tensor = query_projection_weight.shape[0] // part_width
    token_rows = normed_hidden_state.reshape(count_rows, part_width)

    down_all = lax.all_gather(adapter_down_maps, "dp", axis=0, tiled=True)
    n_pool = down_all.shape[0] // ADAPTER_RANK

    pieces = gather_tensor(token_rows, "tensor", n_tensor)
    full_rows = jnp.transpose(pieces, (1, 0, 2)).reshape(count_rows, n_tensor * part_width)
    base = jnp.dot(full_rows, query_projection_weight, preferred_element_type=jnp.float32)

    up_local, down_all, base = lax.optimization_barrier((adapter_up_maps, down_all, base))
    up_all = lax.all_gather(up_local, "dp", axis=0, tiled=True)

    position = pool_lookup(adapter_per_request, adapter_pool_position)
    row_position = jnp.tile(position, steps)
    pick = jnp.arange(n_pool, dtype=jnp.int32)[:, None] == row_position[None, :]
    full_t = lax.dot_general(
        down_all, token_rows, (((1,), (1,)), ((), ())), preferred_element_type=jnp.float32
    ).reshape(n_pool, ADAPTER_RANK, count_rows)
    shrink_local = jnp.sum(jnp.where(pick[:, None, :], full_t, 0.0), axis=0)
    partials = gather_tensor(shrink_local, "tensor", n_tensor)
    shrink = partials[0]
    for j in range(1, n_tensor):
        shrink = shrink + partials[j]
    shrink = shrink.astype(jnp.bfloat16)
    wide_t = jnp.where(pick[:, None, :], shrink[None, :, :], jnp.zeros((), jnp.bfloat16))
    delta = lax.dot_general(
        wide_t.reshape(n_pool * ADAPTER_RANK, count_rows),
        up_all,
        (((0,), (0,)), ((), ())),
        preferred_element_type=jnp.float32,
    )
    query = (base + delta).reshape(steps, requests, heads_width).astype(jnp.bfloat16)
    return attend(query, key_value_cache, step_key_value, cache_valid_length)


def solution(mesh):
    return jax.shard_map(
        per_device,
        mesh=mesh,
        in_specs=(
            P(None, "dp", "tensor"),
            P(None, "tensor"),
            P("dp", "tensor"),
            P("dp", "tensor"),
            P(None, "dp", None, "tensor"),
            P(None, None, "dp", "tensor"),
            P("dp"),
            P("dp"),
            P(),
        ),
        out_specs=P(None, "dp", "tensor"),
        check_vma=False,
    )
```

```python
import math

import jax
import jax.numpy as jnp
from jax import lax
from jax.experimental import pallas as pl
from jax.sharding import PartitionSpec as P

HEAD_SIZE = 128
ADAPTER_RANK = 64


def pool_lookup(adapters, adapter_pool_position):
    table = jnp.arange(adapter_pool_position.shape[0], dtype=jnp.int32)
    match = adapters[:, None] == table[None, :]
    return jnp.sum(jnp.where(match, adapter_pool_position[None, :], 0), axis=1)


REQ_BLOCK = 16


def attend_kernel(q_ref, k_ref, v_ref, nk_ref, nv_ref, valid_ref, o_ref):
    scale = 1.0 / math.sqrt(HEAD_SIZE)
    q = q_ref[...]
    keys = k_ref[0]
    values = v_ref[0]
    new_keys = nk_ref[...]
    new_values = nv_ref[...]
    cache_scores = lax.dot_general(
        q, keys, (((2,), (2,)), ((0,), (0,))), preferred_element_type=jnp.float32
    ) * scale
    cache_scores = jnp.where(valid_ref[...] > 0, cache_scores, -1e30)
    fresh_scores = lax.dot_general(
        q, new_keys, (((2,), (2,)), ((0,), (0,))), preferred_element_type=jnp.float32
    ) * scale
    rows = q.shape[1]
    group = rows // new_keys.shape[1]
    row_id = lax.broadcasted_iota(jnp.int32, fresh_scores.shape, 1)
    step_id = lax.broadcasted_iota(jnp.int32, fresh_scores.shape, 2)
    fresh_scores = jnp.where(row_id >= step_id * group, fresh_scores, -1e30)
    top = jnp.maximum(
        jnp.max(cache_scores, axis=-1, keepdims=True), jnp.max(fresh_scores, axis=-1, keepdims=True)
    )
    cache_expo = jnp.exp(cache_scores - top)
    fresh_expo = jnp.exp(fresh_scores - top)
    total = jnp.sum(cache_expo, axis=-1, keepdims=True) + jnp.sum(fresh_expo, axis=-1, keepdims=True)
    mixed = lax.dot_general(
        cache_expo.astype(jnp.bfloat16), values, (((2,), (1,)), ((0,), (0,))),
        preferred_element_type=jnp.float32,
    )
    mixed = mixed + lax.dot_general(
        fresh_expo.astype(jnp.bfloat16), new_values, (((2,), (1,)), ((0,), (0,))),
        preferred_element_type=jnp.float32,
    )
    o_ref[...] = (mixed / total).astype(o_ref.dtype)


def attend(query, key_value_cache, step_key_value, cache_valid_length):
    steps, requests, width = query.shape
    length = key_value_cache.shape[2]
    kv_local = key_value_cache.shape[3] // HEAD_SIZE
    heads = width // HEAD_SIZE
    group = heads // kv_local
    rows = steps * group
    q = query.reshape(steps, requests, kv_local, group, HEAD_SIZE)
    q = jnp.transpose(q, (1, 2, 0, 3, 4)).reshape(requests * kv_local, rows, HEAD_SIZE)
    cache = key_value_cache.reshape(2, requests, length, kv_local, HEAD_SIZE)
    cache = jnp.transpose(cache, (0, 1, 3, 2, 4)).reshape(2, requests * kv_local, length, HEAD_SIZE)
    fresh = step_key_value.reshape(steps, 2, requests, kv_local, HEAD_SIZE)
    fresh = jnp.transpose(fresh, (1, 2, 3, 0, 4)).reshape(2, requests * kv_local, steps, HEAD_SIZE)
    valid = jnp.arange(length, dtype=jnp.int32)[None, :] < cache_valid_length[:, None]
    valid = jnp.repeat(valid.astype(jnp.int32), kv_local, axis=0)[:, None, :]
    batch = requests * kv_local
    blk = min(REQ_BLOCK, batch)
    out = pl.pallas_call(
        attend_kernel,
        grid=(batch // blk,),
        in_specs=[
            pl.BlockSpec((blk, rows, HEAD_SIZE), lambda i: (i, 0, 0)),
            pl.BlockSpec((1, blk, length, HEAD_SIZE), lambda i: (0, i, 0, 0)),
            pl.BlockSpec((1, blk, length, HEAD_SIZE), lambda i: (1, i, 0, 0)),
            pl.BlockSpec((blk, steps, HEAD_SIZE), lambda i: (i, 0, 0)),
            pl.BlockSpec((blk, steps, HEAD_SIZE), lambda i: (i, 0, 0)),
            pl.BlockSpec((blk, 1, length), lambda i: (i, 0, 0)),
        ],
        out_specs=pl.BlockSpec((blk, rows, HEAD_SIZE), lambda i: (i, 0, 0)),
        out_shape=jax.ShapeDtypeStruct((batch, rows, HEAD_SIZE), query.dtype),
    )(q, cache, cache, fresh[0], fresh[1], valid)
    out = out.reshape(requests, kv_local, steps, group, HEAD_SIZE)
    return jnp.transpose(out, (2, 0, 1, 3, 4)).reshape(steps, requests, width)


def gather_tensor(value, axis_name, count):
    tiled = jnp.broadcast_to(value[None], (count,) + value.shape)
    return lax.all_to_all(tiled, axis_name, 0, 0, tiled=True)


def per_device(
    normed_hidden_state,
    query_projection_weight,
    adapter_down_maps,
    adapter_up_maps,
    key_value_cache,
    step_key_value,
    cache_valid_length,
    adapter_per_request,
    adapter_pool_position,
):
    steps, requests, part_width = normed_hidden_state.shape
    count_rows = steps * requests
    heads_width = query_projection_weight.shape[1]
    n_tensor = query_projection_weight.shape[0] // part_width
    token_rows = normed_hidden_state.reshape(count_rows, part_width)

    down_all = lax.all_gather(adapter_down_maps, "dp", axis=0, tiled=True)
    n_pool = down_all.shape[0] // ADAPTER_RANK

    pieces = gather_tensor(token_rows, "tensor", n_tensor)
    full_rows = jnp.transpose(pieces, (1, 0, 2)).reshape(count_rows, n_tensor * part_width)
    base = jnp.dot(full_rows, query_projection_weight, preferred_element_type=jnp.float32)

    up_local, down_all, base = lax.optimization_barrier((adapter_up_maps, down_all, base))
    up_all = lax.all_gather(up_local, "dp", axis=0, tiled=True)

    position = pool_lookup(adapter_per_request, adapter_pool_position)
    row_position = jnp.tile(position, steps)
    pick = jnp.arange(n_pool, dtype=jnp.int32)[:, None] == row_position[None, :]
    full_t = lax.dot_general(
        down_all, token_rows, (((1,), (1,)), ((), ())), preferred_element_type=jnp.float32
    ).reshape(n_pool, ADAPTER_RANK, count_rows)
    shrink_local = jnp.sum(jnp.where(pick[:, None, :], full_t, 0.0), axis=0)
    partials = gather_tensor(shrink_local, "tensor", n_tensor)
    shrink = partials[0]
    for j in range(1, n_tensor):
        shrink = shrink + partials[j]
    shrink = shrink.astype(jnp.bfloat16)
    wide_t = jnp.where(pick[:, None, :], shrink[None, :, :], jnp.zeros((), jnp.bfloat16))
    delta = lax.dot_general(
        wide_t.reshape(n_pool * ADAPTER_RANK, count_rows),
        up_all,
        (((0,), (0,)), ((), ())),
        preferred_element_type=jnp.float32,
    )
    query = (base + delta).reshape(steps, requests, heads_width).astype(jnp.bfloat16)
    return attend(query, key_value_cache, step_key_value, cache_valid_length)


def solution(mesh):
    return jax.shard_map(
        per_device,
        mesh=mesh,
        in_specs=(
            P(None, "dp", "tensor"),
            P(None, "tensor"),
            P("dp", "tensor"),
            P("dp", "tensor"),
            P(None, "dp", None, "tensor"),
            P(None, None, "dp", "tensor"),
            P("dp"),
            P("dp"),
            P(),
        ),
        out_specs=P(None, "dp", "tensor"),
        check_vma=False,
    )
```

```python
import math

import jax
import jax.numpy as jnp
from jax import lax
from jax.experimental import pallas as pl
from jax.sharding import PartitionSpec as P

HEAD_SIZE = 128
ADAPTER_RANK = 64


def pool_lookup(adapters, adapter_pool_position):
    table = jnp.arange(adapter_pool_position.shape[0], dtype=jnp.int32)
    match = adapters[:, None] == table[None, :]
    return jnp.sum(jnp.where(match, adapter_pool_position[None, :], 0), axis=1)


def attend_kernel(q_ref, kt_ref, v_ref, lens_ref, o_ref):
    scale = 1.0 / math.sqrt(HEAD_SIZE)
    q = q_ref[...]
    scores = lax.dot_general(
        q, kt_ref[...], (((2,), (1,)), ((0,), (0,))), preferred_element_type=jnp.float32
    ) * scale
    length = v_ref.shape[1] // 2
    rows = q.shape[1]
    col = lax.broadcasted_iota(jnp.int32, scores.shape, 2)
    row = lax.broadcasted_iota(jnp.int32, scores.shape, 1)
    fresh = col - length
    group = rows // 4
    limit = jnp.broadcast_to(lens_ref[...], scores.shape)
    valid = ((col < length) & (col < limit)) | ((col >= length) & (fresh < 4) & (row >= fresh * group))
    scores = jnp.where(valid, scores, -1e30)
    top = jnp.max(scores, axis=-1, keepdims=True)
    expo = jnp.exp(scores - top)
    total = jnp.sum(expo, axis=-1, keepdims=True)
    mixed = lax.dot_general(
        expo.astype(jnp.bfloat16), v_ref[...], (((2,), (1,)), ((0,), (0,))),
        preferred_element_type=jnp.float32,
    )
    o_ref[...] = (mixed / total).astype(o_ref.dtype)


def prepare_keys(key_value_cache, step_key_value, cache_valid_length):
    _, requests, length, width = key_value_cache.shape
    steps = step_key_value.shape[0]
    kv_local = width // HEAD_SIZE
    batch = requests * kv_local
    cache = key_value_cache.reshape(2, requests, length, kv_local, HEAD_SIZE)
    cache = jnp.transpose(cache, (0, 1, 3, 2, 4)).reshape(2, batch, length, HEAD_SIZE)
    fresh = step_key_value.reshape(steps, 2, requests, kv_local, HEAD_SIZE)
    fresh = jnp.transpose(fresh, (1, 2, 3, 0, 4)).reshape(2, batch, steps, HEAD_SIZE)
    pad = jnp.zeros((2, batch, length - steps, HEAD_SIZE), fresh.dtype)
    ext = jnp.concatenate([cache, fresh, pad], axis=2)
    keys_t = jnp.transpose(ext[0], (0, 2, 1))
    lens = jnp.repeat(cache_valid_length, kv_local)
    lens = jnp.broadcast_to(lens[:, None, None], (batch, 1, 2 * length)).astype(jnp.int32)
    return keys_t, ext[1], lens


def attend(query, keys_t, values, lens, blk=32):
    steps, requests, width = query.shape
    batch, _, keys = keys_t.shape
    kv_local = batch // requests
    group = width // HEAD_SIZE // kv_local
    rows = steps * group
    q = query.reshape(steps, requests, kv_local, group, HEAD_SIZE)
    q = jnp.transpose(q, (1, 2, 0, 3, 4)).reshape(batch, rows, HEAD_SIZE)
    blk = min(blk, batch)
    out = pl.pallas_call(
        attend_kernel,
        grid=(batch // blk,),
        in_specs=[
            pl.BlockSpec((blk, rows, HEAD_SIZE), lambda i: (i, 0, 0)),
            pl.BlockSpec((blk, HEAD_SIZE, keys), lambda i: (i, 0, 0)),
            pl.BlockSpec((blk, keys, HEAD_SIZE), lambda i: (i, 0, 0)),
            pl.BlockSpec((blk, 1, keys), lambda i: (i, 0, 0)),
        ],
        out_specs=pl.BlockSpec((blk, rows, HEAD_SIZE), lambda i: (i, 0, 0)),
        out_shape=jax.ShapeDtypeStruct((batch, rows, HEAD_SIZE), query.dtype),
    )(q, keys_t, values, lens)
    out = out.reshape(requests, kv_local, steps, group, HEAD_SIZE)
    return jnp.transpose(out, (2, 0, 1, 3, 4)).reshape(steps, requests, width)


def gather_tensor(value, axis_name, count):
    tiled = jnp.broadcast_to(value[None], (count,) + value.shape)
    return lax.all_to_all(tiled, axis_name, 0, 0, tiled=True)


def per_device(
    normed_hidden_state,
    query_projection_weight,
    adapter_down_maps,
    adapter_up_maps,
    key_value_cache,
    step_key_value,
    cache_valid_length,
    adapter_per_request,
    adapter_pool_position,
):
    steps, requests, part_width = normed_hidden_state.shape
    count_rows = steps * requests
    heads_width = query_projection_weight.shape[1]
    n_tensor = query_projection_weight.shape[0] // part_width
    token_rows = normed_hidden_state.reshape(count_rows, part_width)

    down_all = lax.all_gather(adapter_down_maps, "dp", axis=0, tiled=True)
    n_pool = down_all.shape[0] // ADAPTER_RANK

    pieces = gather_tensor(token_rows, "tensor", n_tensor)
    full_rows = jnp.transpose(pieces, (1, 0, 2)).reshape(count_rows, n_tensor * part_width)
    base = jnp.dot(full_rows, query_projection_weight, preferred_element_type=jnp.float32)

    up_local, down_all, base = lax.optimization_barrier((adapter_up_maps, down_all, base))
    up_all = lax.all_gather(up_local, "dp", axis=0, tiled=True)

    position = pool_lookup(adapter_per_request, adapter_pool_position)
    row_position = jnp.tile(position, steps)
    pick = jnp.arange(n_pool, dtype=jnp.int32)[:, None] == row_position[None, :]
    full_t = lax.dot_general(
        down_all, token_rows, (((1,), (1,)), ((), ())), preferred_element_type=jnp.float32
    ).reshape(n_pool, ADAPTER_RANK, count_rows)
    shrink_local = jnp.sum(jnp.where(pick[:, None, :], full_t, 0.0), axis=0)
    partials = gather_tensor(shrink_local, "tensor", n_tensor)
    shrink = partials[0]
    for j in range(1, n_tensor):
        shrink = shrink + partials[j]
    shrink = shrink.astype(jnp.bfloat16)
    wide_t = jnp.where(pick[:, None, :], shrink[None, :, :], jnp.zeros((), jnp.bfloat16))
    delta = lax.dot_general(
        wide_t.reshape(n_pool * ADAPTER_RANK, count_rows),
        up_all,
        (((0,), (0,)), ((), ())),
        preferred_element_type=jnp.float32,
    )
    query = (base + delta).reshape(steps, requests, heads_width).astype(jnp.bfloat16)
    keys_t, values, lens = prepare_keys(key_value_cache, step_key_value, cache_valid_length)
    return attend(query, keys_t, values, lens)


def solution(mesh):
    return jax.shard_map(
        per_device,
        mesh=mesh,
        in_specs=(
            P(None, "dp", "tensor"),
            P(None, "tensor"),
            P("dp", "tensor"),
            P("dp", "tensor"),
            P(None, "dp", None, "tensor"),
            P(None, None, "dp", "tensor"),
            P("dp"),
            P("dp"),
            P(),
        ),
        out_specs=P(None, "dp", "tensor"),
        check_vma=False,
    )
```

```python
import math

import jax
import jax.numpy as jnp
from jax import lax
from jax.sharding import PartitionSpec as P

HEAD_SIZE = 128
ADAPTER_RANK = 64


def pool_lookup(adapters, adapter_pool_position):
    table = jnp.arange(adapter_pool_position.shape[0], dtype=jnp.int32)
    match = adapters[:, None] == table[None, :]
    return jnp.sum(jnp.where(match, adapter_pool_position[None, :], 0), axis=1)


def attend(query, key_value_cache, step_key_value, cache_valid_length):
    steps = step_key_value.shape[0]
    requests = step_key_value.shape[2]
    length = key_value_cache.shape[2]
    kv_local = key_value_cache.shape[3] // HEAD_SIZE
    group = query.shape[2] // HEAD_SIZE // kv_local
    scale = 1.0 / math.sqrt(HEAD_SIZE)
    grouped = query.reshape(steps, requests, kv_local, group, HEAD_SIZE)
    keys = key_value_cache[0].reshape(requests, length, kv_local, HEAD_SIZE)
    values = key_value_cache[1].reshape(requests, length, kv_local, HEAD_SIZE)
    new_keys = step_key_value[:, 0].reshape(steps, requests, kv_local, HEAD_SIZE)
    new_values = step_key_value[:, 1].reshape(steps, requests, kv_local, HEAD_SIZE)
    cache_scores = (
        jnp.einsum("trkgd,rckd->trkgc", grouped, keys, preferred_element_type=jnp.float32) * scale
    )
    valid = jnp.arange(length, dtype=jnp.int32)[None, :] < cache_valid_length[:, None]
    cache_scores = jnp.where(valid[None, :, None, None, :], cache_scores, -1e30)
    fresh_scores = (
        jnp.einsum("trkgd,srkd->trkgs", grouped, new_keys, preferred_element_type=jnp.float32)
        * scale
    )
    causal = (
        jnp.arange(steps, dtype=jnp.int32)[:, None] >= jnp.arange(steps, dtype=jnp.int32)[None, :]
    )
    fresh_scores = jnp.where(causal[:, None, None, None, :], fresh_scores, -1e30)
    top = jnp.maximum(jnp.max(cache_scores, axis=-1), jnp.max(fresh_scores, axis=-1))
    cache_expo = jnp.exp(cache_scores - top[..., None])
    fresh_expo = jnp.exp(fresh_scores - top[..., None])
    total = jnp.sum(cache_expo, axis=-1) + jnp.sum(fresh_expo, axis=-1)
    mixed = jnp.einsum(
        "trkgc,rckd->trkgd",
        cache_expo.astype(jnp.bfloat16),
        values,
        preferred_element_type=jnp.float32,
    )
    mixed = mixed + jnp.einsum(
        "trkgs,srkd->trkgd",
        fresh_expo.astype(jnp.bfloat16),
        new_values,
        preferred_element_type=jnp.float32,
    )
    attended = mixed / total[..., None]
    return attended.reshape(steps, requests, -1).astype(jnp.bfloat16)


def gather_tensor(value, axis_name, count):
    tiled = jnp.broadcast_to(value[None], (count,) + value.shape)
    return lax.all_to_all(tiled, axis_name, 0, 0, tiled=True)


def per_device(
    normed_hidden_state,
    query_projection_weight,
    adapter_down_maps,
    adapter_up_maps,
    key_value_cache,
    step_key_value,
    cache_valid_length,
    adapter_per_request,
    adapter_pool_position,
):
    steps, requests, part_width = normed_hidden_state.shape
    count_rows = steps * requests
    heads_width = query_projection_weight.shape[1]
    n_tensor = query_projection_weight.shape[0] // part_width
    token_rows = normed_hidden_state.reshape(count_rows, part_width)

    down_all = lax.all_gather(adapter_down_maps, "dp", axis=0, tiled=True)
    n_pool = down_all.shape[0] // ADAPTER_RANK

    pieces = gather_tensor(token_rows, "tensor", n_tensor)
    full_rows = jnp.transpose(pieces, (1, 0, 2)).reshape(count_rows, n_tensor * part_width)
    base = jnp.dot(full_rows, query_projection_weight, preferred_element_type=jnp.float32)

    up_local, down_all, base = lax.optimization_barrier((adapter_up_maps, down_all, base))
    half = heads_width // 2
    up_first = lax.all_gather(up_local[:, :half], "dp", axis=0, tiled=True)
    up_second = lax.all_gather(up_local[:, half:], "dp", axis=0, tiled=True)

    position = pool_lookup(adapter_per_request, adapter_pool_position)
    row_position = jnp.tile(position, steps)
    pick = jnp.arange(n_pool, dtype=jnp.int32)[:, None] == row_position[None, :]
    full_t = lax.dot_general(
        down_all, token_rows, (((1,), (1,)), ((), ())), preferred_element_type=jnp.float32
    ).reshape(n_pool, ADAPTER_RANK, count_rows)
    shrink_local = jnp.sum(jnp.where(pick[:, None, :], full_t, 0.0), axis=0)
    partials = gather_tensor(shrink_local, "tensor", n_tensor)
    shrink = partials[0]
    for j in range(1, n_tensor):
        shrink = shrink + partials[j]
    shrink = shrink.astype(jnp.bfloat16)
    wide_t = jnp.where(pick[:, None, :], shrink[None, :, :], jnp.zeros((), jnp.bfloat16))
    wide_rows = wide_t.reshape(n_pool * ADAPTER_RANK, count_rows)
    def heads(cols, up_part):
        delta = lax.dot_general(
            wide_rows, up_part, (((0,), (0,)), ((), ())), preferred_element_type=jnp.float32
        )
        query = (base[:, cols] + delta).reshape(steps, requests, half).astype(jnp.bfloat16)
        return attend(query, key_value_cache, step_key_value, cache_valid_length)

    first = heads(slice(0, half), up_first)
    first, up_second = lax.optimization_barrier((first, up_second))
    second = heads(slice(half, heads_width), up_second)
    return jnp.concatenate([first, second], axis=-1)

def solution(mesh):
    return jax.shard_map(
        per_device,
        mesh=mesh,
        in_specs=(
            P(None, "dp", "tensor"),
            P(None, "tensor"),
            P("dp", "tensor"),
            P("dp", "tensor"),
            P(None, "dp", None, "tensor"),
            P(None, None, "dp", "tensor"),
            P("dp"),
            P("dp"),
            P(),
        ),
        out_specs=P(None, "dp", "tensor"),
        check_vma=False,
    )
```

```python
import math

import jax
import jax.numpy as jnp
from jax import lax
from jax.sharding import PartitionSpec as P

HEAD_SIZE = 128
ADAPTER_RANK = 64


def pool_lookup(adapters, adapter_pool_position):
    table = jnp.arange(adapter_pool_position.shape[0], dtype=jnp.int32)
    match = adapters[:, None] == table[None, :]
    return jnp.sum(jnp.where(match, adapter_pool_position[None, :], 0), axis=1)


def attend(query, key_value_cache, step_key_value, cache_valid_length):
    steps = step_key_value.shape[0]
    requests = step_key_value.shape[2]
    length = key_value_cache.shape[2]
    kv_local = key_value_cache.shape[3] // HEAD_SIZE
    group = query.shape[2] // HEAD_SIZE // kv_local
    scale = 1.0 / math.sqrt(HEAD_SIZE)
    grouped = query.reshape(steps, requests, kv_local, group, HEAD_SIZE)
    keys = key_value_cache[0].reshape(requests, length, kv_local, HEAD_SIZE)
    values = key_value_cache[1].reshape(requests, length, kv_local, HEAD_SIZE)
    new_keys = step_key_value[:, 0].reshape(steps, requests, kv_local, HEAD_SIZE)
    new_values = step_key_value[:, 1].reshape(steps, requests, kv_local, HEAD_SIZE)
    cache_scores = (
        jnp.einsum("trkgd,rckd->trkgc", grouped, keys, preferred_element_type=jnp.float32) * scale
    )
    valid = jnp.arange(length, dtype=jnp.int32)[None, :] < cache_valid_length[:, None]
    cache_scores = jnp.where(valid[None, :, None, None, :], cache_scores, -1e30)
    fresh_scores = (
        jnp.einsum("trkgd,srkd->trkgs", grouped, new_keys, preferred_element_type=jnp.float32)
        * scale
    )
    causal = (
        jnp.arange(steps, dtype=jnp.int32)[:, None] >= jnp.arange(steps, dtype=jnp.int32)[None, :]
    )
    fresh_scores = jnp.where(causal[:, None, None, None, :], fresh_scores, -1e30)
    top = jnp.maximum(jnp.max(cache_scores, axis=-1), jnp.max(fresh_scores, axis=-1))
    cache_expo = jnp.exp(cache_scores - top[..., None])
    fresh_expo = jnp.exp(fresh_scores - top[..., None])
    total = jnp.sum(cache_expo, axis=-1) + jnp.sum(fresh_expo, axis=-1)
    mixed = jnp.einsum(
        "trkgc,rckd->trkgd",
        cache_expo.astype(jnp.bfloat16),
        values,
        preferred_element_type=jnp.float32,
    )
    mixed = mixed + jnp.einsum(
        "trkgs,srkd->trkgd",
        fresh_expo.astype(jnp.bfloat16),
        new_values,
        preferred_element_type=jnp.float32,
    )
    attended = mixed / total[..., None]
    return attended.reshape(steps, requests, -1).astype(jnp.bfloat16)


def gather_tensor(value, axis_name, count):
    tiled = jnp.broadcast_to(value[None], (count,) + value.shape)
    return lax.all_to_all(tiled, axis_name, 0, 0, tiled=True)


def per_device(
    normed_hidden_state,
    query_projection_weight,
    adapter_down_maps,
    adapter_up_maps,
    key_value_cache,
    step_key_value,
    cache_valid_length,
    adapter_per_request,
    adapter_pool_position,
):
    steps, requests, part_width = normed_hidden_state.shape
    count_rows = steps * requests
    heads_width = query_projection_weight.shape[1]
    n_tensor = query_projection_weight.shape[0] // part_width
    token_rows = normed_hidden_state.reshape(count_rows, part_width)

    down_all = lax.all_gather(adapter_down_maps, "dp", axis=0, tiled=True)
    n_pool = down_all.shape[0] // ADAPTER_RANK

    def base_rows(rows):
        pieces = gather_tensor(rows, "tensor", n_tensor)
        full_rows = jnp.transpose(pieces, (1, 0, 2)).reshape(rows.shape[0], n_tensor * part_width)
        return jnp.dot(full_rows, query_projection_weight, preferred_element_type=jnp.float32)

    split = count_rows // 2
    base_first = base_rows(token_rows[:split])

    up_local, down_all, base_first = lax.optimization_barrier(
        (adapter_up_maps, down_all, base_first)
    )
    up_all = lax.all_gather(up_local, "dp", axis=0, tiled=True)
    base = jnp.concatenate([base_first, base_rows(token_rows[split:])], axis=0)

    position = pool_lookup(adapter_per_request, adapter_pool_position)
    row_position = jnp.tile(position, steps)
    pick = jnp.arange(n_pool, dtype=jnp.int32)[:, None] == row_position[None, :]
    full_t = lax.dot_general(
        down_all, token_rows, (((1,), (1,)), ((), ())), preferred_element_type=jnp.float32
    ).reshape(n_pool, ADAPTER_RANK, count_rows)
    shrink_local = jnp.sum(jnp.where(pick[:, None, :], full_t, 0.0), axis=0)
    partials = gather_tensor(shrink_local, "tensor", n_tensor)
    shrink = partials[0]
    for j in range(1, n_tensor):
        shrink = shrink + partials[j]
    shrink = shrink.astype(jnp.bfloat16)
    wide_t = jnp.where(pick[:, None, :], shrink[None, :, :], jnp.zeros((), jnp.bfloat16))
    delta = lax.dot_general(
        wide_t.reshape(n_pool * ADAPTER_RANK, count_rows),
        up_all,
        (((0,), (0,)), ((), ())),
        preferred_element_type=jnp.float32,
    )
    query = (base + delta).reshape(steps, requests, heads_width).astype(jnp.bfloat16)
    return attend(query, key_value_cache, step_key_value, cache_valid_length)


def solution(mesh):
    return jax.shard_map(
        per_device,
        mesh=mesh,
        in_specs=(
            P(None, "dp", "tensor"),
            P(None, "tensor"),
            P("dp", "tensor"),
            P("dp", "tensor"),
            P(None, "dp", None, "tensor"),
            P(None, None, "dp", "tensor"),
            P("dp"),
            P("dp"),
            P(),
        ),
        out_specs=P(None, "dp", "tensor"),
        check_vma=False,
    )
```

```python
import math

import jax
import jax.numpy as jnp
from jax import lax
from jax.sharding import PartitionSpec as P

HEAD_SIZE = 128
ADAPTER_RANK = 64


def pool_lookup(adapters, adapter_pool_position):
    table = jnp.arange(adapter_pool_position.shape[0], dtype=jnp.int32)
    match = adapters[:, None] == table[None, :]
    return jnp.sum(jnp.where(match, adapter_pool_position[None, :], 0), axis=1)


def attend(query, key_value_cache, step_key_value, cache_valid_length):
    steps = step_key_value.shape[0]
    requests = step_key_value.shape[2]
    length = key_value_cache.shape[2]
    kv_local = key_value_cache.shape[3] // HEAD_SIZE
    group = query.shape[2] // HEAD_SIZE // kv_local
    scale = 1.0 / math.sqrt(HEAD_SIZE)
    grouped = query.reshape(steps, requests, kv_local, group, HEAD_SIZE)
    keys = key_value_cache[0].reshape(requests, length, kv_local, HEAD_SIZE)
    values = key_value_cache[1].reshape(requests, length, kv_local, HEAD_SIZE)
    new_keys = step_key_value[:, 0].reshape(steps, requests, kv_local, HEAD_SIZE)
    new_values = step_key_value[:, 1].reshape(steps, requests, kv_local, HEAD_SIZE)
    cache_scores = (
        jnp.einsum("trkgd,rckd->trkgc", grouped, keys, preferred_element_type=jnp.float32) * scale
    )
    valid = jnp.arange(length, dtype=jnp.int32)[None, :] < cache_valid_length[:, None]
    cache_scores = jnp.where(valid[None, :, None, None, :], cache_scores, -1e30)
    fresh_scores = (
        jnp.einsum("trkgd,srkd->trkgs", grouped, new_keys, preferred_element_type=jnp.float32)
        * scale
    )
    causal = (
        jnp.arange(steps, dtype=jnp.int32)[:, None] >= jnp.arange(steps, dtype=jnp.int32)[None, :]
    )
    fresh_scores = jnp.where(causal[:, None, None, None, :], fresh_scores, -1e30)
    top = jnp.maximum(jnp.max(cache_scores, axis=-1), jnp.max(fresh_scores, axis=-1))
    cache_expo = jnp.exp(cache_scores - top[..., None])
    fresh_expo = jnp.exp(fresh_scores - top[..., None])
    total = jnp.sum(cache_expo, axis=-1) + jnp.sum(fresh_expo, axis=-1)
    mixed = jnp.einsum(
        "trkgc,rckd->trkgd",
        cache_expo.astype(jnp.bfloat16),
        values,
        preferred_element_type=jnp.float32,
    )
    mixed = mixed + jnp.einsum(
        "trkgs,srkd->trkgd",
        fresh_expo.astype(jnp.bfloat16),
        new_values,
        preferred_element_type=jnp.float32,
    )
    attended = mixed / total[..., None]
    return attended.reshape(steps, requests, -1).astype(jnp.bfloat16)


def gather_tensor(value, axis_name, count):
    tiled = jnp.broadcast_to(value[None], (count,) + value.shape)
    return lax.all_to_all(tiled, axis_name, 0, 0, tiled=True)


def per_device(
    normed_hidden_state,
    query_projection_weight,
    adapter_down_maps,
    adapter_up_maps,
    key_value_cache,
    step_key_value,
    cache_valid_length,
    adapter_per_request,
    adapter_pool_position,
):
    steps, requests, part_width = normed_hidden_state.shape
    count_rows = steps * requests
    heads_width = query_projection_weight.shape[1]
    n_tensor = query_projection_weight.shape[0] // part_width
    token_rows = normed_hidden_state.reshape(count_rows, part_width)

    down_width = adapter_down_maps.shape[1]
    both = jnp.concatenate([adapter_down_maps, adapter_up_maps], axis=1)
    both_all = lax.all_gather(both, "dp", axis=0, tiled=True)
    down_all = both_all[:, :down_width]
    up_all = both_all[:, down_width:]
    n_pool = down_all.shape[0] // ADAPTER_RANK

    pieces = gather_tensor(token_rows, "tensor", n_tensor)
    full_rows = jnp.transpose(pieces, (1, 0, 2)).reshape(count_rows, n_tensor * part_width)
    base = jnp.dot(full_rows, query_projection_weight, preferred_element_type=jnp.float32)
    lengths_in, base = lax.optimization_barrier((cache_valid_length, base))
    lengths_all = lax.all_gather(lengths_in, "dp", axis=0, tiled=True)


    position = pool_lookup(adapter_per_request, adapter_pool_position)
    row_position = jnp.tile(position, steps)
    pick = jnp.arange(n_pool, dtype=jnp.int32)[:, None] == row_position[None, :]
    full_t = lax.dot_general(
        down_all, token_rows, (((1,), (1,)), ((), ())), preferred_element_type=jnp.float32
    ).reshape(n_pool, ADAPTER_RANK, count_rows)
    shrink_local = jnp.sum(jnp.where(pick[:, None, :], full_t, 0.0), axis=0)
    partials = gather_tensor(shrink_local, "tensor", n_tensor)
    shrink = partials[0]
    for j in range(1, n_tensor):
        shrink = shrink + partials[j]
    shrink = shrink.astype(jnp.bfloat16)
    wide_t = jnp.where(pick[:, None, :], shrink[None, :, :], jnp.zeros((), jnp.bfloat16))
    delta = lax.dot_general(
        wide_t.reshape(n_pool * ADAPTER_RANK, count_rows),
        up_all,
        (((0,), (0,)), ((), ())),
        preferred_element_type=jnp.float32,
    )
    query = (base + delta).reshape(steps, requests, heads_width).astype(jnp.bfloat16)
    query, lengths_all = lax.optimization_barrier((query, lengths_all))
    return attend(query, key_value_cache, step_key_value, cache_valid_length)


def solution(mesh):
    return jax.shard_map(
        per_device,
        mesh=mesh,
        in_specs=(
            P(None, "dp", "tensor"),
            P(None, "tensor"),
            P("dp", "tensor"),
            P("dp", "tensor"),
            P(None, "dp", None, "tensor"),
            P(None, None, "dp", "tensor"),
            P("dp"),
            P("dp"),
            P(),
        ),
        out_specs=P(None, "dp", "tensor"),
        check_vma=False,
    )
```

```python
import math

import jax
import jax.numpy as jnp
from jax import lax
from jax.sharding import PartitionSpec as P

HEAD_SIZE = 128
ADAPTER_RANK = 64


def pool_lookup(adapters, adapter_pool_position):
    table = jnp.arange(adapter_pool_position.shape[0], dtype=jnp.int32)
    match = adapters[:, None] == table[None, :]
    return jnp.sum(jnp.where(match, adapter_pool_position[None, :], 0), axis=1)


def attend(query, key_value_cache, step_key_value, cache_valid_length):
    steps = step_key_value.shape[0]
    requests = step_key_value.shape[2]
    length = key_value_cache.shape[2]
    kv_local = key_value_cache.shape[3] // HEAD_SIZE
    group = query.shape[2] // HEAD_SIZE // kv_local
    scale = 1.0 / math.sqrt(HEAD_SIZE)
    grouped = query.reshape(steps, requests, kv_local, group, HEAD_SIZE)
    keys = key_value_cache[0].reshape(requests, length, kv_local, HEAD_SIZE)
    values = key_value_cache[1].reshape(requests, length, kv_local, HEAD_SIZE)
    new_keys = step_key_value[:, 0].reshape(steps, requests, kv_local, HEAD_SIZE)
    new_values = step_key_value[:, 1].reshape(steps, requests, kv_local, HEAD_SIZE)
    cache_scores = (
        jnp.einsum("trkgd,rckd->trkgc", grouped, keys, preferred_element_type=jnp.float32) * scale
    )
    valid = jnp.arange(length, dtype=jnp.int32)[None, :] < cache_valid_length[:, None]
    cache_scores = jnp.where(valid[None, :, None, None, :], cache_scores, -1e30)
    fresh_scores = (
        jnp.einsum("trkgd,srkd->trkgs", grouped, new_keys, preferred_element_type=jnp.float32)
        * scale
    )
    causal = (
        jnp.arange(steps, dtype=jnp.int32)[:, None] >= jnp.arange(steps, dtype=jnp.int32)[None, :]
    )
    fresh_scores = jnp.where(causal[:, None, None, None, :], fresh_scores, -1e30)
    top = jnp.maximum(jnp.max(cache_scores, axis=-1), jnp.max(fresh_scores, axis=-1))
    cache_expo = jnp.exp(cache_scores - top[..., None])
    fresh_expo = jnp.exp(fresh_scores - top[..., None])
    total = jnp.sum(cache_expo, axis=-1) + jnp.sum(fresh_expo, axis=-1)
    mixed = jnp.einsum(
        "trkgc,rckd->trkgd",
        cache_expo.astype(jnp.bfloat16),
        values,
        preferred_element_type=jnp.float32,
    )
    mixed = mixed + jnp.einsum(
        "trkgs,srkd->trkgd",
        fresh_expo.astype(jnp.bfloat16),
        new_values,
        preferred_element_type=jnp.float32,
    )
    attended = mixed / total[..., None]
    return attended.reshape(steps, requests, -1).astype(jnp.bfloat16)


def gather_tensor(value, axis_name, count):
    tiled = jnp.broadcast_to(value[None], (count,) + value.shape)
    return lax.all_to_all(tiled, axis_name, 0, 0, tiled=True)


def per_device(
    normed_hidden_state,
    query_projection_weight,
    adapter_down_maps,
    adapter_up_maps,
    key_value_cache,
    step_key_value,
    cache_valid_length,
    adapter_per_request,
    adapter_pool_position,
):
    steps, requests, part_width = normed_hidden_state.shape
    count_rows = steps * requests
    heads_width = query_projection_weight.shape[1]
    n_tensor = query_projection_weight.shape[0] // part_width
    token_rows = normed_hidden_state.reshape(count_rows, part_width)

    down_rows, down_width = adapter_down_maps.shape
    up_rows = adapter_up_maps.size // down_width
    both = jnp.concatenate([adapter_down_maps, adapter_up_maps.reshape(up_rows, down_width)], axis=0)
    both_all = lax.all_gather(both, "dp", axis=0, tiled=False)
    n_holders = both_all.shape[0]
    down_all = both_all[:, :down_rows].reshape(n_holders * down_rows, down_width)
    up_all = both_all[:, down_rows:].reshape(n_holders * down_rows, heads_width)
    n_pool = down_all.shape[0] // ADAPTER_RANK

    pieces = gather_tensor(token_rows, "tensor", n_tensor)
    full_rows = jnp.transpose(pieces, (1, 0, 2)).reshape(count_rows, n_tensor * part_width)
    base = jnp.dot(full_rows, query_projection_weight, preferred_element_type=jnp.float32)
    lengths_in, base = lax.optimization_barrier((cache_valid_length, base))
    lengths_all = lax.all_gather(lengths_in, "dp", axis=0, tiled=True)


    position = pool_lookup(adapter_per_request, adapter_pool_position)
    row_position = jnp.tile(position, steps)
    pick = jnp.arange(n_pool, dtype=jnp.int32)[:, None] == row_position[None, :]
    full_t = lax.dot_general(
        down_all, token_rows, (((1,), (1,)), ((), ())), preferred_element_type=jnp.float32
    ).reshape(n_pool, ADAPTER_RANK, count_rows)
    shrink_local = jnp.sum(jnp.where(pick[:, None, :], full_t, 0.0), axis=0)
    partials = gather_tensor(shrink_local, "tensor", n_tensor)
    shrink = partials[0]
    for j in range(1, n_tensor):
        shrink = shrink + partials[j]
    shrink = shrink.astype(jnp.bfloat16)
    wide_t = jnp.where(pick[:, None, :], shrink[None, :, :], jnp.zeros((), jnp.bfloat16))
    delta = lax.dot_general(
        wide_t.reshape(n_pool * ADAPTER_RANK, count_rows),
        up_all,
        (((0,), (0,)), ((), ())),
        preferred_element_type=jnp.float32,
    )
    query = (base + delta).reshape(steps, requests, heads_width).astype(jnp.bfloat16)
    query, lengths_all = lax.optimization_barrier((query, lengths_all))
    return attend(query, key_value_cache, step_key_value, cache_valid_length)


def solution(mesh):
    return jax.shard_map(
        per_device,
        mesh=mesh,
        in_specs=(
            P(None, "dp", "tensor"),
            P(None, "tensor"),
            P("dp", "tensor"),
            P("dp", "tensor"),
            P(None, "dp", None, "tensor"),
            P(None, None, "dp", "tensor"),
            P("dp"),
            P("dp"),
            P(),
        ),
        out_specs=P(None, "dp", "tensor"),
        check_vma=False,
    )
```

```python
import math

import jax
import jax.numpy as jnp
from jax import lax
from jax.sharding import PartitionSpec as P

HEAD_SIZE = 128
ADAPTER_RANK = 64


def pool_lookup(adapters, adapter_pool_position):
    table = jnp.arange(adapter_pool_position.shape[0], dtype=jnp.int32)
    match = adapters[:, None] == table[None, :]
    return jnp.sum(jnp.where(match, adapter_pool_position[None, :], 0), axis=1)


def attend(query, key_value_cache, step_key_value, cache_valid_length):
    steps = step_key_value.shape[0]
    requests = step_key_value.shape[2]
    length = key_value_cache.shape[2]
    kv_local = key_value_cache.shape[3] // HEAD_SIZE
    group = query.shape[2] // HEAD_SIZE // kv_local
    scale = 1.0 / math.sqrt(HEAD_SIZE)
    grouped = query.reshape(steps, requests, kv_local, group, HEAD_SIZE)
    keys = key_value_cache[0].reshape(requests, length, kv_local, HEAD_SIZE)
    values = key_value_cache[1].reshape(requests, length, kv_local, HEAD_SIZE)
    new_keys = step_key_value[:, 0].reshape(steps, requests, kv_local, HEAD_SIZE)
    new_values = step_key_value[:, 1].reshape(steps, requests, kv_local, HEAD_SIZE)
    cache_scores = (
        jnp.einsum("trkgd,rckd->trkgc", grouped, keys, preferred_element_type=jnp.float32) * scale
    )
    valid = jnp.arange(length, dtype=jnp.int32)[None, :] < cache_valid_length[:, None]
    cache_scores = jnp.where(valid[None, :, None, None, :], cache_scores, -1e30)
    fresh_scores = (
        jnp.einsum("trkgd,srkd->trkgs", grouped, new_keys, preferred_element_type=jnp.float32)
        * scale
    )
    causal = (
        jnp.arange(steps, dtype=jnp.int32)[:, None] >= jnp.arange(steps, dtype=jnp.int32)[None, :]
    )
    fresh_scores = jnp.where(causal[:, None, None, None, :], fresh_scores, -1e30)
    top = jnp.maximum(jnp.max(cache_scores, axis=-1), jnp.max(fresh_scores, axis=-1))
    cache_expo = jnp.exp(cache_scores - top[..., None])
    fresh_expo = jnp.exp(fresh_scores - top[..., None])
    total = jnp.sum(cache_expo, axis=-1) + jnp.sum(fresh_expo, axis=-1)
    mixed = jnp.einsum(
        "trkgc,rckd->trkgd",
        cache_expo.astype(jnp.bfloat16),
        values,
        preferred_element_type=jnp.float32,
    )
    mixed = mixed + jnp.einsum(
        "trkgs,srkd->trkgd",
        fresh_expo.astype(jnp.bfloat16),
        new_values,
        preferred_element_type=jnp.float32,
    )
    attended = mixed / total[..., None]
    return attended.reshape(steps, requests, -1).astype(jnp.bfloat16)


def gather_tensor(value, axis_name, count):
    tiled = jnp.broadcast_to(value[None], (count,) + value.shape)
    return lax.all_to_all(tiled, axis_name, 0, 0, tiled=True)


def per_device(
    normed_hidden_state,
    query_projection_weight,
    adapter_down_maps,
    adapter_up_maps,
    key_value_cache,
    step_key_value,
    cache_valid_length,
    adapter_per_request,
    adapter_pool_position,
):
    steps, requests, part_width = normed_hidden_state.shape
    count_rows = steps * requests
    heads_width = query_projection_weight.shape[1]
    n_tensor = query_projection_weight.shape[0] // part_width
    token_rows = normed_hidden_state.reshape(count_rows, part_width)

    down_width = adapter_down_maps.shape[1]
    both = jnp.concatenate([adapter_down_maps, adapter_up_maps], axis=1)
    both_all = lax.all_gather(both, "dp", axis=0, tiled=True)
    down_all = both_all[:, :down_width]
    up_all = both_all[:, down_width:]
    n_pool = down_all.shape[0] // ADAPTER_RANK

    pieces = gather_tensor(token_rows, "tensor", n_tensor)
    full_rows = jnp.transpose(pieces, (1, 0, 2)).reshape(count_rows, n_tensor * part_width)
    base = jnp.dot(full_rows, query_projection_weight, preferred_element_type=jnp.float32)
    lengths_in, base = lax.optimization_barrier((cache_valid_length, base))
    lengths_all = lax.all_gather(lengths_in, "dp", axis=0, tiled=True)


    position = pool_lookup(adapter_per_request, adapter_pool_position)
    row_position = jnp.tile(position, steps)
    pick = jnp.arange(n_pool, dtype=jnp.int32)[:, None] == row_position[None, :]
    full_t = lax.dot_general(
        down_all, token_rows, (((1,), (1,)), ((), ())), preferred_element_type=jnp.float32
    ).reshape(n_pool, ADAPTER_RANK, count_rows)
    shrink_local = jnp.sum(jnp.where(pick[:, None, :], full_t, 0.0), axis=0)
    partials = gather_tensor(shrink_local, "tensor", n_tensor)
    shrink = partials[0]
    for j in range(1, n_tensor):
        shrink = shrink + partials[j]
    shrink = shrink.astype(jnp.bfloat16)
    wide_t = jnp.where(pick[:, None, :], shrink[None, :, :], jnp.zeros((), jnp.bfloat16))
    delta = lax.dot_general(
        wide_t.reshape(n_pool * ADAPTER_RANK, count_rows),
        up_all,
        (((0,), (0,)), ((), ())),
        preferred_element_type=jnp.float32,
    )
    query = (base + delta).reshape(steps, requests, heads_width).astype(jnp.bfloat16)
    lengths_mine = lax.dynamic_slice_in_dim(lengths_all, lax.axis_index("dp") * requests, requests)
    return attend(query, key_value_cache, step_key_value, lengths_mine)


def solution(mesh):
    return jax.shard_map(
        per_device,
        mesh=mesh,
        in_specs=(
            P(None, "dp", "tensor"),
            P(None, "tensor"),
            P("dp", "tensor"),
            P("dp", "tensor"),
            P(None, "dp", None, "tensor"),
            P(None, None, "dp", "tensor"),
            P("dp"),
            P("dp"),
            P(),
        ),
        out_specs=P(None, "dp", "tensor"),
        check_vma=False,
    )
```

```python
import math

import jax
import jax.numpy as jnp
from jax import lax
from jax.sharding import PartitionSpec as P

HEAD_SIZE = 128
ADAPTER_RANK = 64


def pool_lookup(adapters, adapter_pool_position):
    table = jnp.arange(adapter_pool_position.shape[0], dtype=jnp.int32)
    match = adapters[:, None] == table[None, :]
    return jnp.sum(jnp.where(match, adapter_pool_position[None, :], 0), axis=1)


def attend(query, key_value_cache, step_key_value, cache_valid_length):
    steps = step_key_value.shape[0]
    requests = step_key_value.shape[2]
    length = key_value_cache.shape[2]
    kv_local = key_value_cache.shape[3] // HEAD_SIZE
    group = query.shape[2] // HEAD_SIZE // kv_local
    scale = 1.0 / math.sqrt(HEAD_SIZE)
    grouped = query.reshape(steps, requests, kv_local, group, HEAD_SIZE)
    keys = key_value_cache[0].reshape(requests, length, kv_local, HEAD_SIZE)
    values = key_value_cache[1].reshape(requests, length, kv_local, HEAD_SIZE)
    new_keys = step_key_value[:, 0].reshape(steps, requests, kv_local, HEAD_SIZE)
    new_values = step_key_value[:, 1].reshape(steps, requests, kv_local, HEAD_SIZE)
    cache_scores = (
        jnp.einsum("trkgd,rckd->trkgc", grouped, keys, preferred_element_type=jnp.float32) * scale
    )
    valid = jnp.arange(length, dtype=jnp.int32)[None, :] < cache_valid_length[:, None]
    cache_scores = jnp.where(valid[None, :, None, None, :], cache_scores, -1e30)
    fresh_scores = (
        jnp.einsum("trkgd,srkd->trkgs", grouped, new_keys, preferred_element_type=jnp.float32)
        * scale
    )
    causal = (
        jnp.arange(steps, dtype=jnp.int32)[:, None] >= jnp.arange(steps, dtype=jnp.int32)[None, :]
    )
    fresh_scores = jnp.where(causal[:, None, None, None, :], fresh_scores, -1e30)
    top = jnp.maximum(jnp.max(cache_scores, axis=-1), jnp.max(fresh_scores, axis=-1))
    cache_expo = jnp.exp(cache_scores - top[..., None])
    fresh_expo = jnp.exp(fresh_scores - top[..., None])
    total = jnp.sum(cache_expo, axis=-1) + jnp.sum(fresh_expo, axis=-1)
    mixed = jnp.einsum(
        "trkgc,rckd->trkgd",
        cache_expo.astype(jnp.bfloat16),
        values,
        preferred_element_type=jnp.float32,
    )
    mixed = mixed + jnp.einsum(
        "trkgs,srkd->trkgd",
        fresh_expo.astype(jnp.bfloat16),
        new_values,
        preferred_element_type=jnp.float32,
    )
    attended = mixed / total[..., None]
    return attended.reshape(steps, requests, -1).astype(jnp.bfloat16)


def gather_tensor(value, axis_name, count):
    tiled = jnp.broadcast_to(value[None], (count,) + value.shape)
    return lax.all_to_all(tiled, axis_name, 0, 0, tiled=True)


def per_device(
    normed_hidden_state,
    query_projection_weight,
    adapter_down_maps,
    adapter_up_maps,
    key_value_cache,
    step_key_value,
    cache_valid_length,
    adapter_per_request,
    adapter_pool_position,
):
    steps, requests, part_width = normed_hidden_state.shape
    count_rows = steps * requests
    heads_width = query_projection_weight.shape[1]
    n_tensor = query_projection_weight.shape[0] // part_width
    token_rows = normed_hidden_state.reshape(count_rows, part_width)

    down_width = adapter_down_maps.shape[1]
    both = jnp.concatenate([adapter_down_maps, adapter_up_maps], axis=1)
    both_all = lax.all_gather(both, "dp", axis=0, tiled=True)
    down_all = both_all[:, :down_width]
    up_all = both_all[:, down_width:]
    n_pool = down_all.shape[0] // ADAPTER_RANK

    pieces = gather_tensor(token_rows, "tensor", n_tensor)
    full_rows = jnp.transpose(pieces, (1, 0, 2)).reshape(count_rows, n_tensor * part_width)
    base = jnp.dot(full_rows, query_projection_weight, preferred_element_type=jnp.float32)
    lengths_in, base = lax.optimization_barrier((cache_valid_length, base))
    lengths_all = lax.all_gather(lengths_in, "dp", axis=0, tiled=True)


    position = pool_lookup(adapter_per_request, adapter_pool_position)
    row_position = jnp.tile(position, steps)
    pick = jnp.arange(n_pool, dtype=jnp.int32)[:, None] == row_position[None, :]
    padded_rows = jnp.pad(token_rows, ((0, 0), (0, both_all.shape[1] - down_width)))
    full_t = lax.dot_general(
        both_all, padded_rows, (((1,), (1,)), ((), ())), preferred_element_type=jnp.float32
    ).reshape(n_pool, ADAPTER_RANK, count_rows)
    shrink_local = jnp.sum(jnp.where(pick[:, None, :], full_t, 0.0), axis=0)
    partials = gather_tensor(shrink_local, "tensor", n_tensor)
    shrink = partials[0]
    for j in range(1, n_tensor):
        shrink = shrink + partials[j]
    shrink = shrink.astype(jnp.bfloat16)
    wide_t = jnp.where(pick[:, None, :], shrink[None, :, :], jnp.zeros((), jnp.bfloat16))
    delta = lax.dot_general(
        wide_t.reshape(n_pool * ADAPTER_RANK, count_rows),
        up_all,
        (((0,), (0,)), ((), ())),
        preferred_element_type=jnp.float32,
    )
    query = (base + delta).reshape(steps, requests, heads_width).astype(jnp.bfloat16)
    lengths_mine = lax.dynamic_slice_in_dim(lengths_all, lax.axis_index("dp") * requests, requests)
    return attend(query, key_value_cache, step_key_value, lengths_mine)


def solution(mesh):
    return jax.shard_map(
        per_device,
        mesh=mesh,
        in_specs=(
            P(None, "dp", "tensor"),
            P(None, "tensor"),
            P("dp", "tensor"),
            P("dp", "tensor"),
            P(None, "dp", None, "tensor"),
            P(None, None, "dp", "tensor"),
            P("dp"),
            P("dp"),
            P(),
        ),
        out_specs=P(None, "dp", "tensor"),
        check_vma=False,
    )
```
